32 devices in a mesh: tensor: 4 (over x, core), replica: 4 (over z), fsdp: 2 (over y).
Axes of the slice: x: 2, y: 2, z: 4, core: 2. Of those that a mesh axis runs over, the one named last changes fastest.
Arguments:
- gradients: bfloat16 [4, 128, 28672], P('replica', 'fsdp', 'tensor'), may hold values from -6 to 6
- seeds: int32 [2], replicated, may hold values from 0 to 1073741823
- adam_step: int32 [1], replicated, may hold values from 1 to 8
- first_moment: float32 [128, 28672], P(('fsdp', 'replica'), 'tensor'), may hold values from -0.6 to 0.6
- second_moment: float32 [128, 28672], P(('fsdp', 'replica'), 'tensor'), may hold values from 0.001 to 0.1
Outputs:
- new_first: float32 [128, 28672], P(('fsdp', 'replica'), 'tensor')
- new_second: float32 [128, 28672], P(('fsdp', 'replica'), 'tensor')
- step_update: float32 [128, 28672], P(('fsdp', 'replica'), 'tensor')
The draws below stay inside these ranges and needn't reach their ends.
All inputs are finite; a program needn't handle non-finite values.
Results may differ from the reference program's by a relative error of at most 0.012.
The reference program's roundings to bfloat16 on the way (of `projection` and `sketch_rounded`) count: a program that leaves them out, or rounds other values in their place, can miss the bound.
Values may be sent and summed in bfloat16 or wider, within the bound.
No kernel may reach another device: no remote copies, remote signals or barrier semaphores. Data moves between devices by JAX's collectives and lax.ppermute only.
A program may use at most 64 MiB of HBM per device.

```python
import math
import jax
import jax.numpy as jnp
from jax import lax

FF = 28672
RANK = 512
ROWS = 128
N_REPLICA = 4


def block_scale(own_key, shape, pieces, smallest, top_value):
    def one(dim, shards_of):
        steps = jax.random.uniform(jax.random.fold_in(jax.random.fold_in(own_key, 6), dim), (shards_of,), jnp.float32, smallest / len(pieces), top_value / len(pieces))
        return jnp.repeat(jnp.exp(steps), shape[dim] // shards_of).reshape((-1,) + (1,) * (len(shape) - dim - 1))

    factor_of = one(*pieces[0])
    for cut in pieces[1:]:
        factor_of = factor_of * one(*cut)
    return factor_of


def normal_values(stream_key, dims, scale, bound, split=(), held_as=jnp.bfloat16):
    values = jax.random.normal(stream_key, dims, jnp.float32) * scale
    if len(split) > 0:
        values = block_scale(stream_key, dims, split, -0.22, 0.18) * values
    return jnp.clip(values, min=-bound, max=bound).astype(held_as)


def setup_inputs(seed: int = 0) -> dict:
    streams_of = jax.random.split(jax.random.key(seed), 6)
    return {
        "gradients": normal_values(streams_of[0], (N_REPLICA, ROWS, FF), 1.0, 6.0, ((0, 4), (1, 2), (2, 4))),
        "seeds": jax.random.randint(streams_of[1], (2,), 0, 1073741824).astype(jnp.int32),
        "adam_step": jax.random.randint(streams_of[2], (1,), 1, 9).astype(jnp.int32),
        "first_moment": normal_values(streams_of[3], (ROWS, FF), 0.1, 0.6, ((0, 8), (1, 4)), jnp.float32),
        "second_moment": jnp.clip(jnp.exp(math.log(0.1) - 4.6051702 * jax.random.uniform(streams_of[4], (ROWS, FF), jnp.float32) ** block_scale(streams_of[4], (ROWS, FF), ((0, 8), (1, 4)), -0.2, 0.2)), 0.001, 0.1),
    }


def scramble(value):
    value = value ^ lax.shift_right_logical(value, jnp.full_like(value, 16))
    value = value * jnp.int32(-2048144789)
    value = value ^ lax.shift_right_logical(value, jnp.full_like(value, 13))
    value = value * jnp.int32(-1028477387)
    value = value ^ lax.shift_right_logical(value, jnp.full_like(value, 16))
    return value

def projection_block(first_column, columns, rank, seeds):
    seed_key = seeds[0] ^ seeds[1] * jnp.int32(668265263)
    column = lax.broadcasted_iota(jnp.int32, (columns, rank), 0) + first_column
    entry = lax.broadcasted_iota(jnp.int32, (columns, rank), 1)
    counter = (column * jnp.int32(rank) + entry) * jnp.int32(2)
    hash_a = scramble(counter * jnp.int32(-1640531535) ^ seed_key)
    hash_b = scramble((counter + jnp.int32(1)) * jnp.int32(-1640531535) ^ seed_key)
    inverse = 1.0 / 16777216.0
    uniform_a = (lax.shift_right_logical(hash_a, jnp.full_like(hash_a, 8)).astype(jnp.float32) + 0.5) * inverse
    uniform_b = (lax.shift_right_logical(hash_b, jnp.full_like(hash_b, 8)).astype(jnp.float32) + 0.5) * inverse
    gauss = jnp.sqrt(-2.0 * jnp.log(uniform_a)) * jnp.cos(6.283185307179586 * uniform_b)
    return (gauss * rank ** (-0.5)).astype(jnp.bfloat16)

def reference(gradients, seeds, adam_step, first_moment, second_moment):
    projection = projection_block(jnp.int32(0), FF, RANK, seeds)
    wide_proj = projection.astype(jnp.float32)

    def accumulate(total, block):
        return (total + block.astype(jnp.float32), None)
    total, _ = lax.scan(accumulate, jnp.zeros((ROWS, FF), jnp.float32), gradients)
    sketch = jnp.dot(total, wide_proj, precision=lax.Precision.HIGHEST) * (1.0 / N_REPLICA)
    sketch_rounded = sketch.astype(jnp.bfloat16)
    estimate = jnp.dot(sketch_rounded.astype(jnp.float32), wide_proj.T, precision=lax.Precision.HIGHEST)
    new_first = 0.9 * first_moment + 0.1 * estimate
    new_second = 0.95 * second_moment + 0.05 * estimate * estimate
    step_float = adam_step[0].astype(jnp.float32)
    fix_first = 1.0 - jnp.power(jnp.float32(0.9), step_float)
    fix_second = 1.0 - jnp.power(jnp.float32(0.95), step_float)
    step_update = new_first / fix_first / (jnp.sqrt(new_second / fix_second) + 1e-08)
    return (new_first, new_second, step_update)
```

```python
import math

import jax
import jax.numpy as jnp
from jax import lax
from jax.sharding import PartitionSpec as P

RANK = 512
GROUP = ("fsdp", "replica")


def scramble(value):
    value = value ^ lax.shift_right_logical(value, jnp.full_like(value, 16))
    value = value * jnp.int32(-2048144789)
    value = value ^ lax.shift_right_logical(value, jnp.full_like(value, 13))
    value = value * jnp.int32(-1028477387)
    value = value ^ lax.shift_right_logical(value, jnp.full_like(value, 16))
    return value


def projection_block(first_column, columns, rank, seeds):
    seed_key = seeds[0] ^ seeds[1] * jnp.int32(668265263)
    column = lax.broadcasted_iota(jnp.int32, (columns, rank), 0) + first_column
    entry = lax.broadcasted_iota(jnp.int32, (columns, rank), 1)
    counter = (column * jnp.int32(rank) + entry) * jnp.int32(2)
    hash_a = scramble(counter * jnp.int32(-1640531535) ^ seed_key)
    hash_b = scramble((counter + jnp.int32(1)) * jnp.int32(-1640531535) ^ seed_key)
    inverse = 1.0 / 16777216.0
    uniform_a = (
        lax.shift_right_logical(hash_a, jnp.full_like(hash_a, 8)).astype(jnp.float32) + 0.5
    ) * inverse
    uniform_b = (
        lax.shift_right_logical(hash_b, jnp.full_like(hash_b, 8)).astype(jnp.float32) + 0.5
    ) * inverse
    gauss = jnp.sqrt(-2.0 * jnp.log(uniform_a)) * jnp.cos(6.283185307179586 * uniform_b)
    return (gauss * rank ** (-0.5)).astype(jnp.bfloat16)


def adam(first_moment, second_moment, estimate, adam_step):
    new_first = 0.9 * first_moment + 0.1 * estimate
    new_second = 0.95 * second_moment + 0.05 * estimate * estimate
    step_float = adam_step[0].astype(jnp.float32)
    fix_first = 1.0 - jnp.power(jnp.float32(0.9), step_float)
    fix_second = 1.0 - jnp.power(jnp.float32(0.95), step_float)
    step_update = new_first / fix_first / (jnp.sqrt(new_second / fix_second) + 1e-08)
    return (new_first, new_second, step_update)


def per_device_whole(gradients, seeds, adam_step, first_moment, second_moment):
    gradient = gradients[0]
    columns = gradient.shape[1]
    replicas = lax.axis_size("replica")
    column_start = lax.axis_index("tensor") * jnp.int32(columns)
    piece_cols = math.gcd(columns, 512)
    blocks = columns // piece_cols
    starts = column_start + lax.iota(jnp.int32, blocks) * jnp.int32(piece_cols)
    tiles = lax.map(lambda first: projection_block(first, piece_cols, RANK, seeds), starts)
    projection = tiles.reshape(columns, RANK)
    partial_value = jnp.dot(gradient, projection, preferred_element_type=jnp.float32) * (
        1.0 / replicas
    )
    share = lax.psum_scatter(partial_value, "replica", scatter_dimension=0, tiled=True)
    sketch = lax.psum(share, "tensor")
    sketch_rounded = sketch.astype(jnp.bfloat16)
    estimate = lax.dot_general(
        sketch_rounded, projection, (((1,), (1,)), ((), ())), preferred_element_type=jnp.float32
    )
    return adam(first_moment, second_moment, estimate, adam_step)


def per_device(gradients, seeds, adam_step, first_moment, second_moment):
    gradient = gradients[0]
    rows, columns = gradient.shape
    n_fsdp = lax.axis_size("fsdp")
    n_rep = lax.axis_size("replica")
    n_group = n_fsdp * n_rep
    width = columns // n_group
    if columns % (n_group * 128) != 0:
        return per_device_whole(gradients, seeds, adam_step, first_moment, second_moment)
    member = lax.axis_index(GROUP)
    first = lax.axis_index("tensor") * jnp.int32(columns) + member * jnp.int32(width)

    projection = lax.optimization_barrier(projection_block(first, width, RANK, seeds))

    pieces = gradient.reshape(rows, n_group, width).transpose(1, 0, 2)
    held = lax.all_to_all(pieces, GROUP, 0, 0, tiled=True)
    held = held.reshape(n_fsdp, n_rep, rows, width)

    partial_value = None
    for r in range(n_rep):
        term = lax.dot_general(
            held[:, r], projection, (((2,), (0,)), ((), ())),
            preferred_element_type=jnp.float32,
        )
        partial_value = term if partial_value is None else partial_value + term
    partial_value = partial_value.reshape(n_fsdp * rows, RANK) * (1.0 / n_rep)
    sketch = lax.psum(partial_value, ("tensor",) + GROUP)
    sketch_rounded = sketch.astype(jnp.bfloat16)

    estimate = lax.dot_general(
        sketch_rounded, projection, (((1,), (1,)), ((), ())), preferred_element_type=jnp.float32
    )
    out_rows = first_moment.shape[0]
    estimate = estimate.reshape(n_group, out_rows, width)
    estimate = lax.all_to_all(estimate, GROUP, 0, 0, tiled=True)
    estimate = estimate.transpose(1, 0, 2).reshape(out_rows, columns)
    return adam(first_moment, second_moment, estimate, adam_step)


def solution(mesh):
    placed = (
        P("replica", "fsdp", "tensor"),
        P(),
        P(),
        P(("fsdp", "replica"), "tensor"),
        P(("fsdp", "replica"), "tensor"),
    )
    return jax.shard_map(
        per_device,
        mesh=mesh,
        in_specs=placed,
        out_specs=(
            P(("fsdp", "replica"), "tensor"),
            P(("fsdp", "replica"), "tensor"),
            P(("fsdp", "replica"), "tensor"),
        ),
        check_vma=False,
    )
```

```python
import math

import jax
import jax.numpy as jnp
from jax import lax
from jax.sharding import PartitionSpec as P

RANK = 512
GROUP = ("fsdp", "replica")


def scramble(value):
    value = value ^ lax.shift_right_logical(value, jnp.full_like(value, 16))
    value = value * jnp.int32(-2048144789)
    value = value ^ lax.shift_right_logical(value, jnp.full_like(value, 13))
    value = value * jnp.int32(-1028477387)
    value = value ^ lax.shift_right_logical(value, jnp.full_like(value, 16))
    return value


def projection_block(first_column, columns, rank, seeds):
    seed_key = seeds[0] ^ seeds[1] * jnp.int32(668265263)
    column = lax.broadcasted_iota(jnp.int32, (columns, rank), 0) + first_column
    entry = lax.broadcasted_iota(jnp.int32, (columns, rank), 1)
    counter = (column * jnp.int32(rank) + entry) * jnp.int32(2)
    hash_a = scramble(counter * jnp.int32(-1640531535) ^ seed_key)
    hash_b = scramble((counter + jnp.int32(1)) * jnp.int32(-1640531535) ^ seed_key)
    inverse = 1.0 / 16777216.0
    uniform_a = (
        lax.shift_right_logical(hash_a, jnp.full_like(hash_a, 8)).astype(jnp.float32) + 0.5
    ) * inverse
    uniform_b = (
        lax.shift_right_logical(hash_b, jnp.full_like(hash_b, 8)).astype(jnp.float32) + 0.5
    ) * inverse
    gauss = jnp.sqrt(-2.0 * jnp.log(uniform_a)) * jnp.cos(6.283185307179586 * uniform_b)
    return (gauss * rank ** (-0.5)).astype(jnp.bfloat16)


def adam(first_moment, second_moment, estimate, adam_step):
    new_first = 0.9 * first_moment + 0.1 * estimate
    new_second = 0.95 * second_moment + 0.05 * estimate * estimate
    step_float = adam_step[0].astype(jnp.float32)
    fix_first = 1.0 - jnp.power(jnp.float32(0.9), step_float)
    fix_second = 1.0 - jnp.power(jnp.float32(0.95), step_float)
    step_update = new_first / fix_first / (jnp.sqrt(new_second / fix_second) + 1e-08)
    return (new_first, new_second, step_update)


def per_device_whole(gradients, seeds, adam_step, first_moment, second_moment):
    gradient = gradients[0]
    columns = gradient.shape[1]
    replicas = lax.axis_size("replica")
    column_start = lax.axis_index("tensor") * jnp.int32(columns)
    piece_cols = math.gcd(columns, 512)
    blocks = columns // piece_cols
    starts = column_start + lax.iota(jnp.int32, blocks) * jnp.int32(piece_cols)
    tiles = lax.map(lambda first: projection_block(first, piece_cols, RANK, seeds), starts)
    projection = tiles.reshape(columns, RANK)
    partial_value = jnp.dot(gradient, projection, preferred_element_type=jnp.float32) * (
        1.0 / replicas
    )
    share = lax.psum_scatter(partial_value, "replica", scatter_dimension=0, tiled=True)
    sketch = lax.psum(share, "tensor")
    sketch_rounded = sketch.astype(jnp.bfloat16)
    estimate = lax.dot_general(
        sketch_rounded, projection, (((1,), (1,)), ((), ())), preferred_element_type=jnp.float32
    )
    return adam(first_moment, second_moment, estimate, adam_step)


def exchange_sum(value, axes):
    steps = []
    for axis in axes:
        size = lax.axis_size(axis)
        step = 1
        while step < size:
            steps.append((axis, step, [(i, i ^ step) for i in range(size)]))
            step *= 2
    bits = []
    for axis, step, pairs in steps:
        bit = (lax.axis_index(axis) // step) % 2
        half = value.shape[0] // 2
        lower, upper = value[:half], value[half:]
        keep = jnp.where(bit == 0, lower, upper)
        send = jnp.where(bit == 0, upper, lower)
        value = keep + lax.ppermute(send, axis, pairs)
        bits.append(bit)
    for (axis, step, pairs), bit in zip(reversed(steps), reversed(bits)):
        got = lax.ppermute(value, axis, pairs)
        value = jnp.where(
            bit == 0, jnp.concatenate([value, got], 0), jnp.concatenate([got, value], 0)
        )
    return value


def per_device(gradients, seeds, adam_step, first_moment, second_moment):
    gradient = gradients[0]
    rows, columns = gradient.shape
    n_fsdp = lax.axis_size("fsdp")
    n_rep = lax.axis_size("replica")
    n_group = n_fsdp * n_rep
    width = columns // n_group
    if columns % (n_group * 128) != 0:
        return per_device_whole(gradients, seeds, adam_step, first_moment, second_moment)
    member = lax.axis_index(GROUP)
    first = lax.axis_index("tensor") * jnp.int32(columns) + member * jnp.int32(width)

    projection = lax.optimization_barrier(projection_block(first, width, RANK, seeds))

    pieces = gradient.reshape(rows, n_group, width).transpose(1, 0, 2)
    held = lax.all_to_all(pieces, GROUP, 0, 0, tiled=True)
    held = held.reshape(n_fsdp, n_rep, rows, width)

    partial_value = None
    for r in range(n_rep):
        term = lax.dot_general(
            held[:, r], projection, (((2,), (0,)), ((), ())),
            preferred_element_type=jnp.float32,
        )
        partial_value = term if partial_value is None else partial_value + term
    partial_value = partial_value.reshape(n_fsdp * rows, RANK) * (1.0 / n_rep)
    sketch = exchange_sum(partial_value, ("tensor",) + GROUP)
    sketch_rounded = sketch.astype(jnp.bfloat16)

    estimate = lax.dot_general(
        sketch_rounded, projection, (((1,), (1,)), ((), ())), preferred_element_type=jnp.float32
    )
    out_rows = first_moment.shape[0]
    estimate = estimate.reshape(n_group, out_rows, width)
    estimate = lax.all_to_all(estimate, GROUP, 0, 0, tiled=True)
    estimate = estimate.transpose(1, 0, 2).reshape(out_rows, columns)
    return adam(first_moment, second_moment, estimate, adam_step)


def solution(mesh):
    placed = (
        P("replica", "fsdp", "tensor"),
        P(),
        P(),
        P(("fsdp", "replica"), "tensor"),
        P(("fsdp", "replica"), "tensor"),
    )
    return jax.shard_map(
        per_device,
        mesh=mesh,
        in_specs=placed,
        out_specs=(
            P(("fsdp", "replica"), "tensor"),
            P(("fsdp", "replica"), "tensor"),
            P(("fsdp", "replica"), "tensor"),
        ),
        check_vma=False,
    )
```

```python
import math

import jax
import jax.numpy as jnp
from jax import lax
from jax.sharding import PartitionSpec as P

RANK = 512
GROUP = ("fsdp", "replica")
MESH_GROUP = ("replica", "fsdp")


def scramble(value):
    value = value ^ lax.shift_right_logical(value, jnp.full_like(value, 16))
    value = value * jnp.int32(-2048144789)
    value = value ^ lax.shift_right_logical(value, jnp.full_like(value, 13))
    value = value * jnp.int32(-1028477387)
    value = value ^ lax.shift_right_logical(value, jnp.full_like(value, 16))
    return value


def projection_block(first_column, columns, rank, seeds):
    seed_key = seeds[0] ^ seeds[1] * jnp.int32(668265263)
    column = lax.broadcasted_iota(jnp.int32, (columns, rank), 0) + first_column
    entry = lax.broadcasted_iota(jnp.int32, (columns, rank), 1)
    counter = (column * jnp.int32(rank) + entry) * jnp.int32(2)
    hash_a = scramble(counter * jnp.int32(-1640531535) ^ seed_key)
    hash_b = scramble((counter + jnp.int32(1)) * jnp.int32(-1640531535) ^ seed_key)
    inverse = 1.0 / 16777216.0
    uniform_a = (
        lax.shift_right_logical(hash_a, jnp.full_like(hash_a, 8)).astype(jnp.float32) + 0.5
    ) * inverse
    uniform_b = (
        lax.shift_right_logical(hash_b, jnp.full_like(hash_b, 8)).astype(jnp.float32) + 0.5
    ) * inverse
    gauss = jnp.sqrt(-2.0 * jnp.log(uniform_a)) * jnp.cos(6.283185307179586 * uniform_b)
    return (gauss * rank ** (-0.5)).astype(jnp.bfloat16)


def adam(first_moment, second_moment, estimate, adam_step):
    new_first = 0.9 * first_moment + 0.1 * estimate
    new_second = 0.95 * second_moment + 0.05 * estimate * estimate
    step_float = adam_step[0].astype(jnp.float32)
    fix_first = 1.0 - jnp.power(jnp.float32(0.9), step_float)
    fix_second = 1.0 - jnp.power(jnp.float32(0.95), step_float)
    step_update = new_first / fix_first / (jnp.sqrt(new_second / fix_second) + 1e-08)
    return (new_first, new_second, step_update)


def per_device_whole(gradients, seeds, adam_step, first_moment, second_moment):
    gradient = gradients[0]
    columns = gradient.shape[1]
    replicas = lax.axis_size("replica")
    column_start = lax.axis_index("tensor") * jnp.int32(columns)
    piece_cols = math.gcd(columns, 512)
    blocks = columns // piece_cols
    starts = column_start + lax.iota(jnp.int32, blocks) * jnp.int32(piece_cols)
    tiles = lax.map(lambda first: projection_block(first, piece_cols, RANK, seeds), starts)
    projection = tiles.reshape(columns, RANK)
    partial_value = jnp.dot(gradient, projection, preferred_element_type=jnp.float32) * (
        1.0 / replicas
    )
    share = lax.psum_scatter(partial_value, "replica", scatter_dimension=0, tiled=True)
    sketch = lax.psum(share, "tensor")
    sketch_rounded = sketch.astype(jnp.bfloat16)
    estimate = lax.dot_general(
        sketch_rounded, projection, (((1,), (1,)), ((), ())), preferred_element_type=jnp.float32
    )
    return adam(first_moment, second_moment, estimate, adam_step)


def shifted(value_of, axis, size, place=lambda i: i):
    got = [value_of(0)]
    for k in range(1, size):
        pairs = [(place(i), place((i + k) % size)) for i in range(size)]
        got.append(lax.ppermute(value_of(k), axis, pairs))
    return got


def by_source(got, index, size):
    order = (index - jnp.arange(size, dtype=jnp.int32)) % size
    return jnp.take(jnp.stack(got), order, axis=0)


def exchange_sum(value, axes):
    plan = []
    for axis in axes:
        size = lax.axis_size(axis)
        index = lax.axis_index(axis)
        parts = value.reshape(size, value.shape[0] // size, *value.shape[1:])

        def block(k, parts=parts, index=index, size=size):
            return lax.dynamic_index_in_dim(parts, (index + k) % size, 0, keepdims=False)

        got = shifted(block, axis, size)
        value = got[0]
        for term in got[1:]:
            value = value + term
        plan.append((axis, size, index))
    for axis, size, index in reversed(plan):
        got = shifted(lambda k, value=value: value, axis, size)
        value = by_source(got, index, size).reshape(-1, *value.shape[1:])
    return value


def per_device(gradients, seeds, adam_step, first_moment, second_moment):
    gradient = gradients[0]
    rows, columns = gradient.shape
    n_fsdp = lax.axis_size("fsdp")
    n_rep = lax.axis_size("replica")
    n_group = n_fsdp * n_rep
    width = columns // n_group
    if columns % (n_group * 128) != 0:
        return per_device_whole(gradients, seeds, adam_step, first_moment, second_moment)
    member = lax.axis_index(GROUP)
    first = lax.axis_index("tensor") * jnp.int32(columns) + member * jnp.int32(width)

    projection = lax.optimization_barrier(projection_block(first, width, RANK, seeds))

    pieces = gradient.reshape(rows, n_group, width).transpose(1, 0, 2)
    held = lax.all_to_all(pieces, GROUP, 0, 0, tiled=True)
    held = held.reshape(n_fsdp, n_rep, rows, width)
    place = lambda i: (i % n_rep) * n_fsdp + i // n_rep

    partial_value = None
    for r in range(n_rep):
        term = lax.dot_general(
            held[:, r], projection, (((2,), (0,)), ((), ())),
            preferred_element_type=jnp.float32,
        )
        partial_value = term if partial_value is None else partial_value + term
    partial_value = partial_value.reshape(n_fsdp * rows, RANK) * (1.0 / n_rep)
    sketch = exchange_sum(partial_value, ("tensor",) + GROUP)
    sketch_rounded = sketch.astype(jnp.bfloat16)

    estimate = lax.dot_general(
        sketch_rounded, projection, (((1,), (1,)), ((), ())), preferred_element_type=jnp.float32
    )
    out_rows = first_moment.shape[0]
    estimate = estimate.reshape(n_group, out_rows, width)
    got = shifted(lambda k: estimate[(member + k) % n_group], MESH_GROUP, n_group, place)
    estimate = by_source(got, member, n_group).transpose(1, 0, 2).reshape(out_rows, columns)
    return adam(first_moment, second_moment, estimate, adam_step)


def solution(mesh):
    placed = (
        P("replica", "fsdp", "tensor"),
        P(),
        P(),
        P(("fsdp", "replica"), "tensor"),
        P(("fsdp", "replica"), "tensor"),
    )
    return jax.shard_map(
        per_device,
        mesh=mesh,
        in_specs=placed,
        out_specs=(
            P(("fsdp", "replica"), "tensor"),
            P(("fsdp", "replica"), "tensor"),
            P(("fsdp", "replica"), "tensor"),
        ),
        check_vma=False,
    )
```

```python
import math

import jax
import jax.numpy as jnp
from jax import lax
from jax.sharding import PartitionSpec as P

RANK = 512
GROUP = ("fsdp", "replica")
MESH_GROUP = ("replica", "fsdp")


def scramble(value):
    value = value ^ lax.shift_right_logical(value, jnp.full_like(value, 16))
    value = value * jnp.int32(-2048144789)
    value = value ^ lax.shift_right_logical(value, jnp.full_like(value, 13))
    value = value * jnp.int32(-1028477387)
    value = value ^ lax.shift_right_logical(value, jnp.full_like(value, 16))
    return value


def projection_block(first_column, columns, rank, seeds):
    seed_key = seeds[0] ^ seeds[1] * jnp.int32(668265263)
    column = lax.broadcasted_iota(jnp.int32, (columns, rank), 0) + first_column
    entry = lax.broadcasted_iota(jnp.int32, (columns, rank), 1)
    counter = (column * jnp.int32(rank) + entry) * jnp.int32(2)
    hash_a = scramble(counter * jnp.int32(-1640531535) ^ seed_key)
    hash_b = scramble((counter + jnp.int32(1)) * jnp.int32(-1640531535) ^ seed_key)
    inverse = 1.0 / 16777216.0
    uniform_a = (
        lax.shift_right_logical(hash_a, jnp.full_like(hash_a, 8)).astype(jnp.float32) + 0.5
    ) * inverse
    uniform_b = (
        lax.shift_right_logical(hash_b, jnp.full_like(hash_b, 8)).astype(jnp.float32) + 0.5
    ) * inverse
    gauss = jnp.sqrt(-2.0 * jnp.log(uniform_a)) * jnp.cos(6.283185307179586 * uniform_b)
    return (gauss * rank ** (-0.5)).astype(jnp.bfloat16)


def adam(first_moment, second_moment, estimate, adam_step):
    new_first = 0.9 * first_moment + 0.1 * estimate
    new_second = 0.95 * second_moment + 0.05 * estimate * estimate
    step_float = adam_step[0].astype(jnp.float32)
    fix_first = 1.0 - jnp.power(jnp.float32(0.9), step_float)
    fix_second = 1.0 - jnp.power(jnp.float32(0.95), step_float)
    step_update = new_first / fix_first / (jnp.sqrt(new_second / fix_second) + 1e-08)
    return (new_first, new_second, step_update)


def per_device_whole(gradients, seeds, adam_step, first_moment, second_moment):
    gradient = gradients[0]
    columns = gradient.shape[1]
    replicas = lax.axis_size("replica")
    column_start = lax.axis_index("tensor") * jnp.int32(columns)
    piece_cols = math.gcd(columns, 512)
    blocks = columns // piece_cols
    starts = column_start + lax.iota(jnp.int32, blocks) * jnp.int32(piece_cols)
    tiles = lax.map(lambda first: projection_block(first, piece_cols, RANK, seeds), starts)
    projection = tiles.reshape(columns, RANK)
    partial_value = jnp.dot(gradient, projection, preferred_element_type=jnp.float32) * (
        1.0 / replicas
    )
    share = lax.psum_scatter(partial_value, "replica", scatter_dimension=0, tiled=True)
    sketch = lax.psum(share, "tensor")
    sketch_rounded = sketch.astype(jnp.bfloat16)
    estimate = lax.dot_general(
        sketch_rounded, projection, (((1,), (1,)), ((), ())), preferred_element_type=jnp.float32
    )
    return adam(first_moment, second_moment, estimate, adam_step)


def shifted(value_of, axis, size, place=lambda i: i):
    got = [value_of(0)]
    for k in range(1, size):
        pairs = [(place(i), place((i + k) % size)) for i in range(size)]
        got.append(lax.ppermute(value_of(k), axis, pairs))
    return got


def by_source(got, index, size):
    order = (index - jnp.arange(size, dtype=jnp.int32)) % size
    return jnp.take(jnp.stack(got), order, axis=0)


def exchange_sum(value, axes):
    plan = []
    for axis in axes:
        size = lax.axis_size(axis)
        index = lax.axis_index(axis)
        parts = value.reshape(size, value.shape[0] // size, *value.shape[1:])

        def block(k, parts=parts, index=index, size=size):
            return lax.dynamic_index_in_dim(parts, (index + k) % size, 0, keepdims=False)

        got = shifted(block, axis, size)
        value = got[0]
        for term in got[1:]:
            value = value + term
        plan.append((axis, size, index))
    for axis, size, index in reversed(plan):
        got = shifted(lambda k, value=value: value, axis, size)
        value = by_source(got, index, size).reshape(-1, *value.shape[1:])
    return value


def per_device(gradients, seeds, adam_step, first_moment, second_moment):
    gradient = gradients[0]
    rows, columns = gradient.shape
    n_rep = lax.axis_size("replica")
    width = columns // n_rep
    if columns % (n_rep * 128) != 0 or rows % n_rep != 0:
        return per_device_whole(gradients, seeds, adam_step, first_moment, second_moment)
    member = lax.axis_index("replica")
    first = lax.axis_index("tensor") * jnp.int32(columns) + member * jnp.int32(width)

    projection = lax.optimization_barrier(projection_block(first, width, RANK, seeds))

    pieces = gradient.reshape(rows, n_rep, width).transpose(1, 0, 2)
    held = lax.all_to_all(pieces, "replica", 0, 0, tiled=True)

    partial_value = None
    for r in range(n_rep):
        term = jnp.dot(held[r], projection, preferred_element_type=jnp.float32)
        partial_value = term if partial_value is None else partial_value + term
    partial_value = partial_value * (1.0 / n_rep)
    sketch = exchange_sum(partial_value, ("tensor", "replica"))
    sketch_rounded = sketch.astype(jnp.bfloat16)

    estimate = lax.dot_general(
        sketch_rounded, projection, (((1,), (1,)), ((), ())), preferred_element_type=jnp.float32
    )
    out_rows = first_moment.shape[0]
    estimate = estimate.reshape(n_rep, out_rows, width)
    got = shifted(lambda k: estimate[(member + k) % n_rep], "replica", n_rep)
    estimate = by_source(got, member, n_rep).transpose(1, 0, 2).reshape(out_rows, columns)
    return adam(first_moment, second_moment, estimate, adam_step)


def solution(mesh):
    placed = (
        P("replica", "fsdp", "tensor"),
        P(),
        P(),
        P(("fsdp", "replica"), "tensor"),
        P(("fsdp", "replica"), "tensor"),
    )
    return jax.shard_map(
        per_device,
        mesh=mesh,
        in_specs=placed,
        out_specs=(
            P(("fsdp", "replica"), "tensor"),
            P(("fsdp", "replica"), "tensor"),
            P(("fsdp", "replica"), "tensor"),
        ),
        check_vma=False,
    )
```

```python
import math

import jax
import jax.numpy as jnp
from jax import lax
from jax.sharding import PartitionSpec as P

RANK = 512
GROUP = ("fsdp", "replica")
MESH_GROUP = ("replica", "fsdp")


def scramble(value):
    value = value ^ lax.shift_right_logical(value, jnp.full_like(value, 16))
    value = value * jnp.int32(-2048144789)
    value = value ^ lax.shift_right_logical(value, jnp.full_like(value, 13))
    value = value * jnp.int32(-1028477387)
    value = value ^ lax.shift_right_logical(value, jnp.full_like(value, 16))
    return value


def projection_block(first_column, columns, rank, seeds):
    seed_key = seeds[0] ^ seeds[1] * jnp.int32(668265263)
    column = lax.broadcasted_iota(jnp.int32, (columns, rank), 0) + first_column
    entry = lax.broadcasted_iota(jnp.int32, (columns, rank), 1)
    counter = (column * jnp.int32(rank) + entry) * jnp.int32(2)
    hash_a = scramble(counter * jnp.int32(-1640531535) ^ seed_key)
    hash_b = scramble((counter + jnp.int32(1)) * jnp.int32(-1640531535) ^ seed_key)
    inverse = 1.0 / 16777216.0
    uniform_a = (
        lax.shift_right_logical(hash_a, jnp.full_like(hash_a, 8)).astype(jnp.float32) + 0.5
    ) * inverse
    uniform_b = (
        lax.shift_right_logical(hash_b, jnp.full_like(hash_b, 8)).astype(jnp.float32) + 0.5
    ) * inverse
    gauss = jnp.sqrt(-2.0 * jnp.log(uniform_a)) * jnp.cos(6.283185307179586 * uniform_b)
    return (gauss * rank ** (-0.5)).astype(jnp.bfloat16)


def adam(first_moment, second_moment, estimate, adam_step):
    new_first = 0.9 * first_moment + 0.1 * estimate
    new_second = 0.95 * second_moment + 0.05 * estimate * estimate
    step_float = adam_step[0].astype(jnp.float32)
    fix_first = 1.0 - jnp.power(jnp.float32(0.9), step_float)
    fix_second = 1.0 - jnp.power(jnp.float32(0.95), step_float)
    step_update = new_first / fix_first / (jnp.sqrt(new_second / fix_second) + 1e-08)
    return (new_first, new_second, step_update)


def per_device_whole(gradients, seeds, adam_step, first_moment, second_moment):
    gradient = gradients[0]
    columns = gradient.shape[1]
    replicas = lax.axis_size("replica")
    column_start = lax.axis_index("tensor") * jnp.int32(columns)
    piece_cols = math.gcd(columns, 512)
    blocks = columns // piece_cols
    starts = column_start + lax.iota(jnp.int32, blocks) * jnp.int32(piece_cols)
    tiles = lax.map(lambda first: projection_block(first, piece_cols, RANK, seeds), starts)
    projection = tiles.reshape(columns, RANK)
    partial_value = jnp.dot(gradient, projection, preferred_element_type=jnp.float32) * (
        1.0 / replicas
    )
    share = lax.psum_scatter(partial_value, "replica", scatter_dimension=0, tiled=True)
    sketch = lax.psum(share, "tensor")
    sketch_rounded = sketch.astype(jnp.bfloat16)
    estimate = lax.dot_general(
        sketch_rounded, projection, (((1,), (1,)), ((), ())), preferred_element_type=jnp.float32
    )
    return adam(first_moment, second_moment, estimate, adam_step)


def shifted(value_of, axis, size, place=lambda i: i):
    got = [value_of(0)]
    for k in range(1, size):
        pairs = [(place(i), place((i + k) % size)) for i in range(size)]
        got.append(lax.ppermute(value_of(k), axis, pairs))
    return got


def by_source(got, index, size):
    order = (index - jnp.arange(size, dtype=jnp.int32)) % size
    return jnp.take(jnp.stack(got), order, axis=0)


def exchange_sum(value, axes):
    plan = []
    for axis in axes:
        size = lax.axis_size(axis)
        index = lax.axis_index(axis)
        parts = value.reshape(size, value.shape[0] // size, *value.shape[1:])

        def block(k, parts=parts, index=index, size=size):
            return lax.dynamic_index_in_dim(parts, (index + k) % size, 0, keepdims=False)

        got = shifted(block, axis, size)
        value = got[0]
        for term in got[1:]:
            value = value + term
        plan.append((axis, size, index))
    for axis, size, index in reversed(plan):
        got = shifted(lambda k, value=value: value, axis, size)
        value = by_source(got, index, size).reshape(-1, *value.shape[1:])
    return value


def per_device(gradients, seeds, adam_step, first_moment, second_moment):
    gradient = gradients[0]
    rows, columns = gradient.shape
    n_rep = lax.axis_size("replica")
    width = columns // n_rep
    if columns % (n_rep * 128) != 0 or rows % n_rep != 0:
        return per_device_whole(gradients, seeds, adam_step, first_moment, second_moment)
    member = lax.axis_index("replica")
    first = lax.axis_index("tensor") * jnp.int32(columns) + member * jnp.int32(width)

    projection = lax.optimization_barrier(projection_block(first, width, RANK, seeds))

    pieces = gradient.reshape(rows, n_rep, width).transpose(1, 0, 2)
    held = lax.all_to_all(pieces, "replica", 0, 0, tiled=True)

    partial_value = None
    for r in range(n_rep):
        term = jnp.dot(held[r], projection, preferred_element_type=jnp.float32)
        partial_value = term if partial_value is None else partial_value + term
    partial_value = partial_value * (1.0 / n_rep)
    sketch = exchange_sum(partial_value, ("tensor", "replica"))
    sketch_rounded = sketch.astype(jnp.bfloat16)

    estimate = lax.dot_general(
        sketch_rounded, projection, (((1,), (1,)), ((), ())), preferred_element_type=jnp.float32
    )
    out_rows = first_moment.shape[0]
    estimate = estimate.reshape(n_rep, out_rows, width).astype(jnp.bfloat16)
    got = shifted(lambda k: estimate[(member + k) % n_rep], "replica", n_rep)
    estimate = by_source(got, member, n_rep).transpose(1, 0, 2).reshape(out_rows, columns)
    estimate = estimate.astype(jnp.float32)
    return adam(first_moment, second_moment, estimate, adam_step)


def solution(mesh):
    placed = (
        P("replica", "fsdp", "tensor"),
        P(),
        P(),
        P(("fsdp", "replica"), "tensor"),
        P(("fsdp", "replica"), "tensor"),
    )
    return jax.shard_map(
        per_device,
        mesh=mesh,
        in_specs=placed,
        out_specs=(
            P(("fsdp", "replica"), "tensor"),
            P(("fsdp", "replica"), "tensor"),
            P(("fsdp", "replica"), "tensor"),
        ),
        check_vma=False,
    )
```

```python
import math

import jax
import jax.numpy as jnp
from jax import lax
from jax.sharding import PartitionSpec as P

RANK = 512
GROUP = ("fsdp", "replica")
MESH_GROUP = ("replica", "fsdp")


def scramble(value):
    value = value ^ lax.shift_right_logical(value, jnp.full_like(value, 16))
    value = value * jnp.int32(-2048144789)
    value = value ^ lax.shift_right_logical(value, jnp.full_like(value, 13))
    value = value * jnp.int32(-1028477387)
    value = value ^ lax.shift_right_logical(value, jnp.full_like(value, 16))
    return value


def projection_block(first_column, columns, rank, seeds):
    seed_key = seeds[0] ^ seeds[1] * jnp.int32(668265263)
    column = lax.broadcasted_iota(jnp.int32, (columns, rank), 0) + first_column
    entry = lax.broadcasted_iota(jnp.int32, (columns, rank), 1)
    counter = (column * jnp.int32(rank) + entry) * jnp.int32(2)
    hash_a = scramble(counter * jnp.int32(-1640531535) ^ seed_key)
    hash_b = scramble((counter + jnp.int32(1)) * jnp.int32(-1640531535) ^ seed_key)
    inverse = 1.0 / 16777216.0
    uniform_a = (
        lax.shift_right_logical(hash_a, jnp.full_like(hash_a, 8)).astype(jnp.float32) + 0.5
    ) * inverse
    uniform_b = (
        lax.shift_right_logical(hash_b, jnp.full_like(hash_b, 8)).astype(jnp.float32) + 0.5
    ) * inverse
    gauss = jnp.sqrt(-2.0 * jnp.log(uniform_a)) * jnp.cos(6.283185307179586 * uniform_b)
    return (gauss * rank ** (-0.5)).astype(jnp.bfloat16)


def adam(first_moment, second_moment, estimate, adam_step):
    new_first = 0.9 * first_moment + 0.1 * estimate
    new_second = 0.95 * second_moment + 0.05 * estimate * estimate
    step_float = adam_step[0].astype(jnp.float32)
    fix_first = 1.0 - jnp.power(jnp.float32(0.9), step_float)
    fix_second = 1.0 - jnp.power(jnp.float32(0.95), step_float)
    step_update = new_first / fix_first / (jnp.sqrt(new_second / fix_second) + 1e-08)
    return (new_first, new_second, step_update)


def per_device_whole(gradients, seeds, adam_step, first_moment, second_moment):
    gradient = gradients[0]
    columns = gradient.shape[1]
    replicas = lax.axis_size("replica")
    column_start = lax.axis_index("tensor") * jnp.int32(columns)
    piece_cols = math.gcd(columns, 512)
    blocks = columns // piece_cols
    starts = column_start + lax.iota(jnp.int32, blocks) * jnp.int32(piece_cols)
    tiles = lax.map(lambda first: projection_block(first, piece_cols, RANK, seeds), starts)
    projection = tiles.reshape(columns, RANK)
    partial_value = jnp.dot(gradient, projection, preferred_element_type=jnp.float32) * (
        1.0 / replicas
    )
    share = lax.psum_scatter(partial_value, "replica", scatter_dimension=0, tiled=True)
    sketch = lax.psum(share, "tensor")
    sketch_rounded = sketch.astype(jnp.bfloat16)
    estimate = lax.dot_general(
        sketch_rounded, projection, (((1,), (1,)), ((), ())), preferred_element_type=jnp.float32
    )
    return adam(first_moment, second_moment, estimate, adam_step)


def shifted(value_of, axis, size, place=lambda i: i):
    got = [value_of(0)]
    for k in range(1, size):
        pairs = [(place(i), place((i + k) % size)) for i in range(size)]
        got.append(lax.ppermute(value_of(k), axis, pairs))
    return got


def by_source(got, index, size):
    order = (index - jnp.arange(size, dtype=jnp.int32)) % size
    return jnp.take(jnp.stack(got), order, axis=0)


def exchange_sum(value, axes):
    plan = []
    for axis in axes:
        size = lax.axis_size(axis)
        index = lax.axis_index(axis)
        parts = value.reshape(size, value.shape[0] // size, *value.shape[1:])

        def block(k, parts=parts, index=index, size=size):
            return lax.dynamic_index_in_dim(parts, (index + k) % size, 0, keepdims=False)

        got = shifted(block, axis, size)
        value = got[0]
        for term in got[1:]:
            value = value + term
        plan.append((axis, size, index))
    for axis, size, index in reversed(plan):
        got = shifted(lambda k, value=value: value, axis, size)
        value = by_source(got, index, size).reshape(-1, *value.shape[1:])
    return value


def per_device(gradients, seeds, adam_step, first_moment, second_moment):
    gradient = gradients[0]
    rows, columns = gradient.shape
    n_rep = lax.axis_size("replica")
    width = columns // n_rep
    if columns % (n_rep * 128) != 0 or rows % n_rep != 0:
        return per_device_whole(gradients, seeds, adam_step, first_moment, second_moment)
    member = lax.axis_index("replica")
    first = lax.axis_index("tensor") * jnp.int32(columns) + member * jnp.int32(width)

    projection = lax.optimization_barrier(projection_block(first, width, RANK, seeds))

    pieces = jnp.stack([gradient[:, i * width : (i + 1) * width] for i in range(n_rep)])
    held = lax.all_to_all(pieces, "replica", 0, 0, tiled=True)

    partial_value = None
    for r in range(n_rep):
        term = jnp.dot(held[r], projection, preferred_element_type=jnp.float32)
        partial_value = term if partial_value is None else partial_value + term
    partial_value = partial_value * (1.0 / n_rep)
    sketch = exchange_sum(partial_value, ("tensor", "replica"))
    sketch_rounded = sketch.astype(jnp.bfloat16)

    estimate = lax.dot_general(
        sketch_rounded, projection, (((1,), (1,)), ((), ())), preferred_element_type=jnp.float32
    )
    out_rows = first_moment.shape[0]
    estimate = estimate.reshape(n_rep, out_rows, width).astype(jnp.bfloat16)
    got = shifted(lambda k: estimate[(member + k) % n_rep], "replica", n_rep)
    estimate = by_source(got, member, n_rep).transpose(1, 0, 2).reshape(out_rows, columns)
    estimate = estimate.astype(jnp.float32)
    return adam(first_moment, second_moment, estimate, adam_step)


def solution(mesh):
    placed = (
        P("replica", "fsdp", "tensor"),
        P(),
        P(),
        P(("fsdp", "replica"), "tensor"),
        P(("fsdp", "replica"), "tensor"),
    )
    return jax.shard_map(
        per_device,
        mesh=mesh,
        in_specs=placed,
        out_specs=(
            P(("fsdp", "replica"), "tensor"),
            P(("fsdp", "replica"), "tensor"),
            P(("fsdp", "replica"), "tensor"),
        ),
        check_vma=False,
    )
```

```python
import math

import jax
import jax.numpy as jnp
from jax import lax
from jax.sharding import PartitionSpec as P

RANK = 512
GROUP = ("fsdp", "replica")
MESH_GROUP = ("replica", "fsdp")


def scramble(value):
    value = value ^ lax.shift_right_logical(value, jnp.full_like(value, 16))
    value = value * jnp.int32(-2048144789)
    value = value ^ lax.shift_right_logical(value, jnp.full_like(value, 13))
    value = value * jnp.int32(-1028477387)
    value = value ^ lax.shift_right_logical(value, jnp.full_like(value, 16))
    return value


def projection_block(first_column, columns, rank, seeds):
    seed_key = seeds[0] ^ seeds[1] * jnp.int32(668265263)
    column = lax.broadcasted_iota(jnp.int32, (columns, rank), 0) + first_column
    entry = lax.broadcasted_iota(jnp.int32, (columns, rank), 1)
    counter = (column * jnp.int32(rank) + entry) * jnp.int32(2)
    hash_a = scramble(counter * jnp.int32(-1640531535) ^ seed_key)
    hash_b = scramble((counter + jnp.int32(1)) * jnp.int32(-1640531535) ^ seed_key)
    inverse = 1.0 / 16777216.0
    uniform_a = (
        lax.shift_right_logical(hash_a, jnp.full_like(hash_a, 8)).astype(jnp.float32) + 0.5
    ) * inverse
    uniform_b = (
        lax.shift_right_logical(hash_b, jnp.full_like(hash_b, 8)).astype(jnp.float32) + 0.5
    ) * inverse
    gauss = jnp.sqrt(-2.0 * jnp.log(uniform_a)) * jnp.cos(6.283185307179586 * uniform_b)
    return (gauss * rank ** (-0.5)).astype(jnp.bfloat16)


def adam(first_moment, second_moment, estimate, adam_step):
    new_first = 0.9 * first_moment + 0.1 * estimate
    new_second = 0.95 * second_moment + 0.05 * estimate * estimate
    step_float = adam_step[0].astype(jnp.float32)
    fix_first = 1.0 - jnp.power(jnp.float32(0.9), step_float)
    fix_second = 1.0 - jnp.power(jnp.float32(0.95), step_float)
    step_update = new_first / fix_first / (jnp.sqrt(new_second / fix_second) + 1e-08)
    return (new_first, new_second, step_update)


def per_device_whole(gradients, seeds, adam_step, first_moment, second_moment):
    gradient = gradients[0]
    columns = gradient.shape[1]
    replicas = lax.axis_size("replica")
    column_start = lax.axis_index("tensor") * jnp.int32(columns)
    piece_cols = math.gcd(columns, 512)
    blocks = columns // piece_cols
    starts = column_start + lax.iota(jnp.int32, blocks) * jnp.int32(piece_cols)
    tiles = lax.map(lambda first: projection_block(first, piece_cols, RANK, seeds), starts)
    projection = tiles.reshape(columns, RANK)
    partial_value = jnp.dot(gradient, projection, preferred_element_type=jnp.float32) * (
        1.0 / replicas
    )
    share = lax.psum_scatter(partial_value, "replica", scatter_dimension=0, tiled=True)
    sketch = lax.psum(share, "tensor")
    sketch_rounded = sketch.astype(jnp.bfloat16)
    estimate = lax.dot_general(
        sketch_rounded, projection, (((1,), (1,)), ((), ())), preferred_element_type=jnp.float32
    )
    return adam(first_moment, second_moment, estimate, adam_step)


def shifted(value_of, axis, size, place=lambda i: i):
    got = [value_of(0)]
    for k in range(1, size):
        pairs = [(place(i), place((i + k) % size)) for i in range(size)]
        got.append(lax.ppermute(value_of(k), axis, pairs))
    return got


def by_source(got, index, size):
    return jnp.stack([lax.select_n((index - p) % size, *got) for p in range(size)])


def exchange_sum(value, axes):
    plan = []
    for axis in axes:
        size = lax.axis_size(axis)
        index = lax.axis_index(axis)
        parts = value.reshape(size, value.shape[0] // size, *value.shape[1:])

        def block(k, parts=parts, index=index, size=size):
            return lax.dynamic_index_in_dim(parts, (index + k) % size, 0, keepdims=False)

        got = shifted(block, axis, size)
        value = got[0]
        for term in got[1:]:
            value = value + term
        plan.append((axis, size, index))
    for axis, size, index in reversed(plan):
        got = shifted(lambda k, value=value: value, axis, size)
        value = by_source(got, index, size).reshape(-1, *value.shape[1:])
    return value


def per_device(gradients, seeds, adam_step, first_moment, second_moment):
    gradient = gradients[0]
    rows, columns = gradient.shape
    n_rep = lax.axis_size("replica")
    width = columns // n_rep
    if columns % (n_rep * 128) != 0 or rows % n_rep != 0:
        return per_device_whole(gradients, seeds, adam_step, first_moment, second_moment)
    member = lax.axis_index("replica")
    first = lax.axis_index("tensor") * jnp.int32(columns) + member * jnp.int32(width)

    projection = lax.optimization_barrier(projection_block(first, width, RANK, seeds))

    pieces = jnp.stack([gradient[:, i * width : (i + 1) * width] for i in range(n_rep)])
    held = lax.all_to_all(pieces, "replica", 0, 0, tiled=True)

    partial_value = None
    for r in range(n_rep):
        term = jnp.dot(held[r], projection, preferred_element_type=jnp.float32)
        partial_value = term if partial_value is None else partial_value + term
    partial_value = partial_value * (1.0 / n_rep)
    sketch = exchange_sum(partial_value, ("tensor", "replica"))
    sketch_rounded = sketch.astype(jnp.bfloat16)

    estimate = lax.dot_general(
        sketch_rounded, projection, (((1,), (1,)), ((), ())), preferred_element_type=jnp.float32
    )
    out_rows = first_moment.shape[0]
    estimate = estimate.reshape(n_rep, out_rows, width).astype(jnp.bfloat16)
    got = shifted(lambda k: estimate[(member + k) % n_rep], "replica", n_rep)
    estimate = by_source(got, member, n_rep).transpose(1, 0, 2).reshape(out_rows, columns)
    estimate = estimate.astype(jnp.float32)
    return adam(first_moment, second_moment, estimate, adam_step)


def solution(mesh):
    placed = (
        P("replica", "fsdp", "tensor"),
        P(),
        P(),
        P(("fsdp", "replica"), "tensor"),
        P(("fsdp", "replica"), "tensor"),
    )
    return jax.shard_map(
        per_device,
        mesh=mesh,
        in_specs=placed,
        out_specs=(
            P(("fsdp", "replica"), "tensor"),
            P(("fsdp", "replica"), "tensor"),
            P(("fsdp", "replica"), "tensor"),
        ),
        check_vma=False,
    )
```

```python
import math

import jax
import jax.numpy as jnp
from jax import lax
from jax.sharding import PartitionSpec as P

RANK = 512
GROUP = ("fsdp", "replica")
MESH_GROUP = ("replica", "fsdp")


def scramble(value):
    value = value ^ lax.shift_right_logical(value, jnp.full_like(value, 16))
    value = value * jnp.int32(-2048144789)
    value = value ^ lax.shift_right_logical(value, jnp.full_like(value, 13))
    value = value * jnp.int32(-1028477387)
    value = value ^ lax.shift_right_logical(value, jnp.full_like(value, 16))
    return value


def projection_block(first_column, columns, rank, seeds):
    seed_key = seeds[0] ^ seeds[1] * jnp.int32(668265263)
    column = lax.broadcasted_iota(jnp.int32, (columns, rank), 0) + first_column
    entry = lax.broadcasted_iota(jnp.int32, (columns, rank), 1)
    counter = (column * jnp.int32(rank) + entry) * jnp.int32(2)
    hash_a = scramble(counter * jnp.int32(-1640531535) ^ seed_key)
    hash_b = scramble((counter + jnp.int32(1)) * jnp.int32(-1640531535) ^ seed_key)
    inverse = 1.0 / 16777216.0
    uniform_a = (
        lax.shift_right_logical(hash_a, jnp.full_like(hash_a, 8)).astype(jnp.float32) + 0.5
    ) * inverse
    uniform_b = (
        lax.shift_right_logical(hash_b, jnp.full_like(hash_b, 8)).astype(jnp.float32) + 0.5
    ) * inverse
    gauss = jnp.sqrt(-2.0 * jnp.log(uniform_a)) * jnp.cos(6.283185307179586 * uniform_b)
    return (gauss * rank ** (-0.5)).astype(jnp.bfloat16)


def adam(first_moment, second_moment, estimate, adam_step):
    new_first = 0.9 * first_moment + 0.1 * estimate
    new_second = 0.95 * second_moment + 0.05 * estimate * estimate
    step_float = adam_step[0].astype(jnp.float32)
    fix_first = 1.0 - jnp.power(jnp.float32(0.9), step_float)
    fix_second = 1.0 - jnp.power(jnp.float32(0.95), step_float)
    step_update = new_first / fix_first / (jnp.sqrt(new_second / fix_second) + 1e-08)
    return (new_first, new_second, step_update)


def per_device_whole(gradients, seeds, adam_step, first_moment, second_moment):
    gradient = gradients[0]
    columns = gradient.shape[1]
    replicas = lax.axis_size("replica")
    column_start = lax.axis_index("tensor") * jnp.int32(columns)
    piece_cols = math.gcd(columns, 512)
    blocks = columns // piece_cols
    starts = column_start + lax.iota(jnp.int32, blocks) * jnp.int32(piece_cols)
    tiles = lax.map(lambda first: projection_block(first, piece_cols, RANK, seeds), starts)
    projection = tiles.reshape(columns, RANK)
    partial_value = jnp.dot(gradient, projection, preferred_element_type=jnp.float32) * (
        1.0 / replicas
    )
    share = lax.psum_scatter(partial_value, "replica", scatter_dimension=0, tiled=True)
    sketch = lax.psum(share, "tensor")
    sketch_rounded = sketch.astype(jnp.bfloat16)
    estimate = lax.dot_general(
        sketch_rounded, projection, (((1,), (1,)), ((), ())), preferred_element_type=jnp.float32
    )
    return adam(first_moment, second_moment, estimate, adam_step)


def shifted(value_of, axis, size, place=lambda i: i):
    got = [value_of(0)]
    for k in range(1, size):
        pairs = [(place(i), place((i + k) % size)) for i in range(size)]
        got.append(lax.ppermute(value_of(k), axis, pairs))
    return got


def by_source(got, index, size):
    return jnp.stack([lax.select_n((index - p) % size, *got) for p in range(size)])


def exchange_sum(value, axes):
    plan = []
    for axis in axes:
        size = lax.axis_size(axis)
        index = lax.axis_index(axis)
        parts = value.reshape(size, value.shape[0] // size, *value.shape[1:])

        def block(k, parts=parts, index=index, size=size):
            return lax.dynamic_index_in_dim(parts, (index + k) % size, 0, keepdims=False)

        got = shifted(block, axis, size)
        value = got[0]
        for term in got[1:]:
            value = value + term
        plan.append((axis, size, index))
    for axis, size, index in reversed(plan):
        got = shifted(lambda k, value=value: value, axis, size)
        value = by_source(got, index, size).reshape(-1, *value.shape[1:])
    return value


def per_device(gradients, seeds, adam_step, first_moment, second_moment):
    gradient = gradients[0]
    rows, columns = gradient.shape
    n_rep = lax.axis_size("replica")
    width = columns // n_rep
    if columns % (n_rep * 128) != 0 or rows % n_rep != 0:
        return per_device_whole(gradients, seeds, adam_step, first_moment, second_moment)
    member = lax.axis_index("replica")
    first = lax.axis_index("tensor") * jnp.int32(columns) + member * jnp.int32(width)

    projection = lax.optimization_barrier(projection_block(first, width, RANK, seeds))

    pieces = jnp.stack([gradient[:, i * width : (i + 1) * width] for i in range(n_rep)])
    held = lax.all_to_all(pieces, "replica", 0, 0, tiled=True)

    terms = jnp.dot(
        held.reshape(n_rep * rows, width), projection, preferred_element_type=jnp.float32
    ).reshape(n_rep, rows, RANK)
    partial_value = terms[0]
    for r in range(1, n_rep):
        partial_value = partial_value + terms[r]
    partial_value = partial_value * (1.0 / n_rep)
    sketch = exchange_sum(partial_value, ("tensor", "replica"))
    sketch_rounded = sketch.astype(jnp.bfloat16)

    estimate = lax.dot_general(
        sketch_rounded, projection, (((1,), (1,)), ((), ())), preferred_element_type=jnp.float32
    )
    out_rows = first_moment.shape[0]
    estimate = estimate.reshape(n_rep, out_rows, width).astype(jnp.bfloat16)
    got = shifted(lambda k: estimate[(member + k) % n_rep], "replica", n_rep)
    estimate = by_source(got, member, n_rep).transpose(1, 0, 2).reshape(out_rows, columns)
    estimate = estimate.astype(jnp.float32)
    return adam(first_moment, second_moment, estimate, adam_step)


def solution(mesh):
    placed = (
        P("replica", "fsdp", "tensor"),
        P(),
        P(),
        P(("fsdp", "replica"), "tensor"),
        P(("fsdp", "replica"), "tensor"),
    )
    return jax.shard_map(
        per_device,
        mesh=mesh,
        in_specs=placed,
        out_specs=(
            P(("fsdp", "replica"), "tensor"),
            P(("fsdp", "replica"), "tensor"),
            P(("fsdp", "replica"), "tensor"),
        ),
        check_vma=False,
    )
```

```python
import math

import jax
import jax.numpy as jnp
from jax import lax
from jax.sharding import PartitionSpec as P

RANK = 512
GROUP = ("fsdp", "replica")
MESH_GROUP = ("replica", "fsdp")


def scramble(value):
    value = value ^ lax.shift_right_logical(value, jnp.full_like(value, 16))
    value = value * jnp.int32(-2048144789)
    value = value ^ lax.shift_right_logical(value, jnp.full_like(value, 13))
    value = value * jnp.int32(-1028477387)
    value = value ^ lax.shift_right_logical(value, jnp.full_like(value, 16))
    return value


def projection_block(first_column, columns, rank, seeds):
    seed_key = seeds[0] ^ seeds[1] * jnp.int32(668265263)
    column = lax.broadcasted_iota(jnp.int32, (columns, rank), 0) + first_column
    entry = lax.broadcasted_iota(jnp.int32, (columns, rank), 1)
    counter = (column * jnp.int32(rank) + entry) * jnp.int32(2)
    hash_a = scramble(counter * jnp.int32(-1640531535) ^ seed_key)
    hash_b = scramble((counter + jnp.int32(1)) * jnp.int32(-1640531535) ^ seed_key)
    inverse = 1.0 / 16777216.0
    uniform_a = (
        lax.shift_right_logical(hash_a, jnp.full_like(hash_a, 8)).astype(jnp.float32) + 0.5
    ) * inverse
    uniform_b = (
        lax.shift_right_logical(hash_b, jnp.full_like(hash_b, 8)).astype(jnp.float32) + 0.5
    ) * inverse
    gauss = jnp.sqrt(-2.0 * jnp.log(uniform_a)) * jnp.cos(6.283185307179586 * uniform_b)
    return (gauss * rank ** (-0.5)).astype(jnp.bfloat16)


def adam(first_moment, second_moment, estimate, adam_step):
    new_first = 0.9 * first_moment + 0.1 * estimate
    new_second = 0.95 * second_moment + 0.05 * estimate * estimate
    step_float = adam_step[0].astype(jnp.float32)
    fix_first = 1.0 - jnp.power(jnp.float32(0.9), step_float)
    fix_second = 1.0 - jnp.power(jnp.float32(0.95), step_float)
    step_update = new_first / fix_first / (jnp.sqrt(new_second / fix_second) + 1e-08)
    return (new_first, new_second, step_update)


def per_device_whole(gradients, seeds, adam_step, first_moment, second_moment):
    gradient = gradients[0]
    columns = gradient.shape[1]
    replicas = lax.axis_size("replica")
    column_start = lax.axis_index("tensor") * jnp.int32(columns)
    piece_cols = math.gcd(columns, 512)
    blocks = columns // piece_cols
    starts = column_start + lax.iota(jnp.int32, blocks) * jnp.int32(piece_cols)
    tiles = lax.map(lambda first: projection_block(first, piece_cols, RANK, seeds), starts)
    projection = tiles.reshape(columns, RANK)
    partial_value = jnp.dot(gradient, projection, preferred_element_type=jnp.float32) * (
        1.0 / replicas
    )
    share = lax.psum_scatter(partial_value, "replica", scatter_dimension=0, tiled=True)
    sketch = lax.psum(share, "tensor")
    sketch_rounded = sketch.astype(jnp.bfloat16)
    estimate = lax.dot_general(
        sketch_rounded, projection, (((1,), (1,)), ((), ())), preferred_element_type=jnp.float32
    )
    return adam(first_moment, second_moment, estimate, adam_step)


def shifted(value_of, axis, size, place=lambda i: i):
    got = [value_of(0)]
    for k in range(1, size):
        pairs = [(place(i), place((i + k) % size)) for i in range(size)]
        got.append(lax.ppermute(value_of(k), axis, pairs))
    return got


def by_source(got, index, size):
    return jnp.stack([lax.select_n((index - p) % size, *got) for p in range(size)])


def exchange_sum(value, axes):
    plan = []
    for axis in axes:
        size = lax.axis_size(axis)
        index = lax.axis_index(axis)
        parts = value.reshape(size, value.shape[0] // size, *value.shape[1:])

        def block(k, parts=parts, index=index, size=size):
            return lax.dynamic_index_in_dim(parts, (index + k) % size, 0, keepdims=False)

        got = shifted(block, axis, size)
        value = got[0]
        for term in got[1:]:
            value = value + term
        plan.append((axis, size, index))
    for axis, size, index in reversed(plan):
        got = shifted(lambda k, value=value: value, axis, size)
        value = by_source(got, index, size).reshape(-1, *value.shape[1:])
    return value


def per_device(gradients, seeds, adam_step, first_moment, second_moment):
    gradient = gradients[0]
    rows, columns = gradient.shape
    n_rep = lax.axis_size("replica")
    width = columns // n_rep
    if columns % (n_rep * 128) != 0 or rows % n_rep != 0:
        return per_device_whole(gradients, seeds, adam_step, first_moment, second_moment)
    member = lax.axis_index("replica")
    first = lax.axis_index("tensor") * jnp.int32(columns) + member * jnp.int32(width)

    projection = lax.optimization_barrier(projection_block(first, width, RANK, seeds))

    got = shifted(
        lambda k: lax.dynamic_slice_in_dim(gradient, ((member + k) % n_rep) * width, width, 1),
        "replica",
        n_rep,
    )
    held = by_source(got, member, n_rep)

    terms = jnp.dot(
        held.reshape(n_rep * rows, width), projection, preferred_element_type=jnp.float32
    ).reshape(n_rep, rows, RANK)
    partial_value = terms[0]
    for r in range(1, n_rep):
        partial_value = partial_value + terms[r]
    partial_value = partial_value * (1.0 / n_rep)
    sketch = exchange_sum(partial_value, ("tensor", "replica"))
    sketch_rounded = sketch.astype(jnp.bfloat16)

    estimate = lax.dot_general(
        sketch_rounded, projection, (((1,), (1,)), ((), ())), preferred_element_type=jnp.float32
    )
    out_rows = first_moment.shape[0]
    estimate = estimate.reshape(n_rep, out_rows, width).astype(jnp.bfloat16)
    got = shifted(lambda k: estimate[(member + k) % n_rep], "replica", n_rep)
    estimate = by_source(got, member, n_rep).transpose(1, 0, 2).reshape(out_rows, columns)
    estimate = estimate.astype(jnp.float32)
    return adam(first_moment, second_moment, estimate, adam_step)


def solution(mesh):
    placed = (
        P("replica", "fsdp", "tensor"),
        P(),
        P(),
        P(("fsdp", "replica"), "tensor"),
        P(("fsdp", "replica"), "tensor"),
    )
    return jax.shard_map(
        per_device,
        mesh=mesh,
        in_specs=placed,
        out_specs=(
            P(("fsdp", "replica"), "tensor"),
            P(("fsdp", "replica"), "tensor"),
            P(("fsdp", "replica"), "tensor"),
        ),
        check_vma=False,
    )
```

```python
import math

import jax
import jax.numpy as jnp
from jax import lax
from jax.sharding import PartitionSpec as P

RANK = 512
GROUP = ("fsdp", "replica")
MESH_GROUP = ("replica", "fsdp")


def scramble(value):
    value = value ^ lax.shift_right_logical(value, jnp.full_like(value, 16))
    value = value * jnp.int32(-2048144789)
    value = value ^ lax.shift_right_logical(value, jnp.full_like(value, 13))
    value = value * jnp.int32(-1028477387)
    value = value ^ lax.shift_right_logical(value, jnp.full_like(value, 16))
    return value


def projection_block(first_column, columns, rank, seeds):
    scaled = seeds * jnp.array([1, 668265263], jnp.int32)
    seed_key = lax.reduce(scaled, jnp.int32(0), lax.bitwise_xor, (0,))
    column = lax.broadcasted_iota(jnp.int32, (columns, rank), 0) + first_column
    entry = lax.broadcasted_iota(jnp.int32, (columns, rank), 1)
    counter = (column * jnp.int32(rank) + entry) * jnp.int32(2)
    hash_a = scramble(counter * jnp.int32(-1640531535) ^ seed_key)
    hash_b = scramble((counter + jnp.int32(1)) * jnp.int32(-1640531535) ^ seed_key)
    inverse = 1.0 / 16777216.0
    uniform_a = (
        lax.shift_right_logical(hash_a, jnp.full_like(hash_a, 8)).astype(jnp.float32) + 0.5
    ) * inverse
    uniform_b = (
        lax.shift_right_logical(hash_b, jnp.full_like(hash_b, 8)).astype(jnp.float32) + 0.5
    ) * inverse
    gauss = jnp.sqrt(-2.0 * jnp.log(uniform_a)) * jnp.cos(6.283185307179586 * uniform_b)
    return (gauss * rank ** (-0.5)).astype(jnp.bfloat16)


def adam(first_moment, second_moment, estimate, adam_step):
    new_first = 0.9 * first_moment + 0.1 * estimate
    new_second = 0.95 * second_moment + 0.05 * estimate * estimate
    step_float = adam_step[0].astype(jnp.float32)
    fix_first = 1.0 - jnp.power(jnp.float32(0.9), step_float)
    fix_second = 1.0 - jnp.power(jnp.float32(0.95), step_float)
    step_update = new_first / fix_first / (jnp.sqrt(new_second / fix_second) + 1e-08)
    return (new_first, new_second, step_update)


def per_device_whole(gradients, seeds, adam_step, first_moment, second_moment):
    gradient = gradients[0]
    columns = gradient.shape[1]
    replicas = lax.axis_size("replica")
    column_start = lax.axis_index("tensor") * jnp.int32(columns)
    piece_cols = math.gcd(columns, 512)
    blocks = columns // piece_cols
    starts = column_start + lax.iota(jnp.int32, blocks) * jnp.int32(piece_cols)
    tiles = lax.map(lambda first: projection_block(first, piece_cols, RANK, seeds), starts)
    projection = tiles.reshape(columns, RANK)
    partial_value = jnp.dot(gradient, projection, preferred_element_type=jnp.float32) * (
        1.0 / replicas
    )
    share = lax.psum_scatter(partial_value, "replica", scatter_dimension=0, tiled=True)
    sketch = lax.psum(share, "tensor")
    sketch_rounded = sketch.astype(jnp.bfloat16)
    estimate = lax.dot_general(
        sketch_rounded, projection, (((1,), (1,)), ((), ())), preferred_element_type=jnp.float32
    )
    return adam(first_moment, second_moment, estimate, adam_step)


def shifted(value_of, axis, size, place=lambda i: i):
    got = [value_of(0)]
    for k in range(1, size):
        pairs = [(place(i), place((i + k) % size)) for i in range(size)]
        got.append(lax.ppermute(value_of(k), axis, pairs))
    return got


def by_source(got, index, size):
    return jnp.stack([lax.select_n((index - p) % size, *got) for p in range(size)])


def exchange_sum(value, axes):
    plan = []
    for axis in axes:
        size = lax.axis_size(axis)
        index = lax.axis_index(axis)
        parts = value.reshape(size, value.shape[0] // size, *value.shape[1:])

        def block(k, parts=parts, index=index, size=size):
            return lax.dynamic_index_in_dim(parts, (index + k) % size, 0, keepdims=False)

        got = shifted(block, axis, size)
        value = got[0]
        for term in got[1:]:
            value = value + term
        plan.append((axis, size, index))
    for axis, size, index in reversed(plan):
        got = shifted(lambda k, value=value: value, axis, size)
        value = by_source(got, index, size).reshape(-1, *value.shape[1:])
    return value


def per_device(gradients, seeds, adam_step, first_moment, second_moment):
    gradient = gradients[0]
    rows, columns = gradient.shape
    n_rep = lax.axis_size("replica")
    width = columns // n_rep
    if columns % (n_rep * 128) != 0 or rows % n_rep != 0:
        return per_device_whole(gradients, seeds, adam_step, first_moment, second_moment)
    member = lax.axis_index("replica")
    first = lax.axis_index("tensor") * jnp.int32(columns) + member * jnp.int32(width)

    projection = lax.optimization_barrier(projection_block(first, width, RANK, seeds))

    got = shifted(
        lambda k: lax.dynamic_slice_in_dim(gradient, ((member + k) % n_rep) * width, width, 1),
        "replica",
        n_rep,
    )
    held = by_source(got, member, n_rep)

    terms = jnp.dot(
        held.reshape(n_rep * rows, width), projection, preferred_element_type=jnp.float32
    ).reshape(n_rep, rows, RANK)
    partial_value = terms[0]
    for r in range(1, n_rep):
        partial_value = partial_value + terms[r]
    partial_value = partial_value * (1.0 / n_rep)
    sketch = exchange_sum(partial_value, ("tensor", "replica"))
    sketch_rounded = sketch.astype(jnp.bfloat16)

    estimate = lax.dot_general(
        sketch_rounded, projection, (((1,), (1,)), ((), ())), preferred_element_type=jnp.float32
    )
    out_rows = first_moment.shape[0]
    estimate = estimate.reshape(n_rep, out_rows, width).astype(jnp.bfloat16)
    got = shifted(lambda k: estimate[(member + k) % n_rep], "replica", n_rep)
    estimate = by_source(got, member, n_rep).transpose(1, 0, 2).reshape(out_rows, columns)
    estimate = estimate.astype(jnp.float32)
    return adam(first_moment, second_moment, estimate, adam_step)


def solution(mesh):
    placed = (
        P("replica", "fsdp", "tensor"),
        P(),
        P(),
        P(("fsdp", "replica"), "tensor"),
        P(("fsdp", "replica"), "tensor"),
    )
    return jax.shard_map(
        per_device,
        mesh=mesh,
        in_specs=placed,
        out_specs=(
            P(("fsdp", "replica"), "tensor"),
            P(("fsdp", "replica"), "tensor"),
            P(("fsdp", "replica"), "tensor"),
        ),
        check_vma=False,
    )
```

```python
import math

import jax
import jax.numpy as jnp
from jax import lax
from jax.sharding import PartitionSpec as P

RANK = 512
GROUP = ("fsdp", "replica")
MESH_GROUP = ("replica", "fsdp")


def scramble(value):
    value = value ^ lax.shift_right_logical(value, jnp.full_like(value, 16))
    value = value * jnp.int32(-2048144789)
    value = value ^ lax.shift_right_logical(value, jnp.full_like(value, 13))
    value = value * jnp.int32(-1028477387)
    value = value ^ lax.shift_right_logical(value, jnp.full_like(value, 16))
    return value


def projection_block(first_column, columns, rank, seeds):
    scaled = seeds * jnp.array([1, 668265263], jnp.int32)
    seed_key = lax.reduce(scaled, jnp.int32(0), lax.bitwise_xor, (0,))
    column = lax.broadcasted_iota(jnp.int32, (columns, rank), 0) + first_column
    entry = lax.broadcasted_iota(jnp.int32, (columns, rank), 1)
    counter = (column * jnp.int32(rank) + entry) * jnp.int32(2)
    hash_a = scramble(counter * jnp.int32(-1640531535) ^ seed_key)
    hash_b = scramble((counter + jnp.int32(1)) * jnp.int32(-1640531535) ^ seed_key)
    inverse = 1.0 / 16777216.0
    uniform_a = (
        lax.shift_right_logical(hash_a, jnp.full_like(hash_a, 8)).astype(jnp.float32) + 0.5
    ) * inverse
    uniform_b = (
        lax.shift_right_logical(hash_b, jnp.full_like(hash_b, 8)).astype(jnp.float32) + 0.5
    ) * inverse
    gauss = jnp.sqrt(-2.0 * jnp.log(uniform_a)) * jnp.cos(6.283185307179586 * uniform_b)
    return (gauss * rank ** (-0.5)).astype(jnp.bfloat16)


def adam(first_moment, second_moment, estimate, adam_step):
    new_first = 0.9 * first_moment + 0.1 * estimate
    new_second = 0.95 * second_moment + 0.05 * estimate * estimate
    step_float = adam_step[0].astype(jnp.float32)
    fix_first = 1.0 - jnp.power(jnp.float32(0.9), step_float)
    fix_second = 1.0 - jnp.power(jnp.float32(0.95), step_float)
    step_update = new_first / fix_first / (jnp.sqrt(new_second / fix_second) + 1e-08)
    return (new_first, new_second, step_update)


def per_device_whole(gradients, seeds, adam_step, first_moment, second_moment):
    gradient = gradients[0]
    columns = gradient.shape[1]
    replicas = lax.axis_size("replica")
    column_start = lax.axis_index("tensor") * jnp.int32(columns)
    piece_cols = math.gcd(columns, 512)
    blocks = columns // piece_cols
    starts = column_start + lax.iota(jnp.int32, blocks) * jnp.int32(piece_cols)
    tiles = lax.map(lambda first: projection_block(first, piece_cols, RANK, seeds), starts)
    projection = tiles.reshape(columns, RANK)
    partial_value = jnp.dot(gradient, projection, preferred_element_type=jnp.float32) * (
        1.0 / replicas
    )
    share = lax.psum_scatter(partial_value, "replica", scatter_dimension=0, tiled=True)
    sketch = lax.psum(share, "tensor")
    sketch_rounded = sketch.astype(jnp.bfloat16)
    estimate = lax.dot_general(
        sketch_rounded, projection, (((1,), (1,)), ((), ())), preferred_element_type=jnp.float32
    )
    return adam(first_moment, second_moment, estimate, adam_step)


def shifted(value_of, axis, size, place=lambda i: i):
    got = [value_of(0)]
    for k in range(1, size):
        pairs = [(place(i), place((i + k) % size)) for i in range(size)]
        got.append(lax.ppermute(value_of(k), axis, pairs))
    return got


def by_source(got, index, size):
    return jnp.stack([lax.select_n((index - p) % size, *got) for p in range(size)])


def exchange_sum(value, axes):
    plan = []
    for axis in axes:
        size = lax.axis_size(axis)
        index = lax.axis_index(axis)
        parts = value.reshape(size, value.shape[0] // size, *value.shape[1:])

        def block(k, parts=parts, index=index, size=size):
            return lax.dynamic_index_in_dim(parts, (index + k) % size, 0, keepdims=False)

        got = shifted(block, axis, size)
        value = got[0]
        for term in got[1:]:
            value = value + term
        plan.append((axis, size, index))
    for axis, size, index in reversed(plan):
        got = shifted(lambda k, value=value: value, axis, size)
        value = by_source(got, index, size).reshape(-1, *value.shape[1:])
    return value


def per_device(gradients, seeds, adam_step, first_moment, second_moment):
    gradient = gradients[0]
    rows, columns = gradient.shape
    n_rep = lax.axis_size("replica")
    width = columns // n_rep
    if columns % (n_rep * 128) != 0 or rows % n_rep != 0:
        return per_device_whole(gradients, seeds, adam_step, first_moment, second_moment)
    member = lax.axis_index("replica")
    first = lax.axis_index("tensor") * jnp.int32(columns) + member * jnp.int32(width)

    projection = lax.optimization_barrier(projection_block(first, width, RANK, seeds))

    got = shifted(
        lambda k: lax.dynamic_slice_in_dim(gradient, ((member + k) % n_rep) * width, width, 1),
        "replica",
        n_rep,
    )
    held = jnp.stack(got)

    terms = jnp.dot(
        held.reshape(n_rep * rows, width), projection, preferred_element_type=jnp.float32
    ).reshape(n_rep, rows, RANK)
    partial_value = terms[0]
    for r in range(1, n_rep):
        partial_value = partial_value + terms[r]
    partial_value = partial_value * (1.0 / n_rep)
    sketch = exchange_sum(partial_value, ("tensor", "replica"))
    sketch_rounded = sketch.astype(jnp.bfloat16)

    estimate = lax.dot_general(
        sketch_rounded, projection, (((1,), (1,)), ((), ())), preferred_element_type=jnp.float32
    )
    out_rows = first_moment.shape[0]
    estimate = estimate.reshape(n_rep, out_rows, width).astype(jnp.bfloat16)
    got = shifted(lambda k: estimate[(member + k) % n_rep], "replica", n_rep)
    estimate = by_source(got, member, n_rep).transpose(1, 0, 2).reshape(out_rows, columns)
    estimate = estimate.astype(jnp.float32)
    return adam(first_moment, second_moment, estimate, adam_step)


def solution(mesh):
    placed = (
        P("replica", "fsdp", "tensor"),
        P(),
        P(),
        P(("fsdp", "replica"), "tensor"),
        P(("fsdp", "replica"), "tensor"),
    )
    return jax.shard_map(
        per_device,
        mesh=mesh,
        in_specs=placed,
        out_specs=(
            P(("fsdp", "replica"), "tensor"),
            P(("fsdp", "replica"), "tensor"),
            P(("fsdp", "replica"), "tensor"),
        ),
        check_vma=False,
    )
```
